256 devices in a mesh: gx: 16 (over z, core), gy: 4 (over x), gz: 4 (over y).
Axes of the slice: x: 4, y: 4, z: 8, core: 2. Of those that a mesh axis runs over, the one named last changes fastest.
Arguments:
- fields: float32 [5, 512, 256, 512], P(None, 'gx', 'gy', 'gz'), may hold values from -4 to 9
- viscous: float32 [5], replicated, may hold values from 1 to 8000
Outputs:
- updated: float32 [5, 512, 256, 512], P(None, 'gx', 'gy', 'gz')
The draws below stay inside these ranges and needn't reach their ends.
All inputs are finite; a program needn't handle non-finite values.
Results may differ from the reference program's by a relative error of at most 0.0003.
Values sent between devices are 32-bit elements; how exact they have to be, the bound alone decides.
No kernel may reach another device: no remote copies, remote signals or barrier semaphores. Data moves between devices by JAX's collectives and lax.ppermute only.
A program may use at most 128 MiB of HBM per device.

```python
import math
import jax
import jax.numpy as jnp
from jax import lax

NF = 5
NX = 512
NY = 256
NZ = 512


def draw_fields(key, part):
    keys = jax.random.split(jax.random.fold_in(key, 7), 7)
    height = (jnp.arange(NY, dtype=jnp.float32) + 0.5) / NY
    profile = 4.0 * height * (1.0 - height)
    amplitude = jax.random.uniform(keys[0], (NF,), jnp.float32, 0.5, 1.5)
    amplitude = jnp.where(jnp.arange(NF) == 0, amplitude + 4.5, amplitude)
    total = amplitude[:, None, None, None] * profile[None, None, :, None]
    mode_count = 3
    lowest_wave = 3 * NX // 10
    highest_wave = 2 * NX // 5 + 1
    wave_number = jax.random.randint(keys[1], (NF, mode_count), lowest_wave, highest_wave)
    height_wave = jax.random.randint(keys[2], (NF, mode_count), 1, 4)
    height_phase = jax.random.uniform(keys[3], (NF, mode_count), jnp.float32, 0.0, 2.0 * math.pi)
    span_phase = jax.random.uniform(keys[4], (NF, mode_count, NZ), jnp.float32, 0.0, 2.0 * math.pi)
    mode_size = jax.random.uniform(keys[5], (NF, mode_count, NZ), jnp.float32, 0.6, 1.0)
    white = 0.3 * jax.random.normal(keys[6], (NF, NX, NY, NZ), jnp.float32)
    cells = jnp.arange(NX, dtype=jnp.int32)
    rows = jnp.arange(NY, dtype=jnp.int32)
    for mode in range(mode_count):
        turn = jnp.mod(wave_number[:, mode][:, None] * cells[None, :], NX).astype(jnp.float32) * (2.0 * math.pi / NX)
        height_turn = jnp.mod(height_wave[:, mode][:, None] * rows[None, :], NY).astype(jnp.float32) * (2.0 * math.pi / NY)
        envelope = 0.75 + 0.25 * jnp.cos(height_turn + height_phase[:, mode][:, None])
        wave = mode_size[:, mode][:, None, :] * jnp.sin(turn[:, :, None] + span_phase[:, mode][:, None, :])
        total = total + wave[:, :, None, :] * envelope[:, None, :, None]
    return jnp.clip(total + white, -4.0, 9.0)


def draw_viscous(key, part):
    keys = jax.random.split(jax.random.fold_in(key, 13), 3)
    rates = jnp.exp(jax.random.uniform(keys[0], (NF,), jnp.float32, 0.0, math.log(8000.0)))
    pick = jax.random.randint(keys[1], (), 0, NF)
    slots = jnp.arange(NF, dtype=jnp.int32)
    low_rate = jax.random.uniform(keys[2], (), jnp.float32, 1.0, 2.0)
    return jnp.where(slots == pick, low_rate, rates)


def setup_inputs(seed: int = 0) -> dict:
    streams_of = jax.random.split(jax.random.key(seed), 3)
    fields = draw_fields(jax.random.fold_in(streams_of[2], 71), 0)
    viscous = draw_viscous(jax.random.fold_in(streams_of[2], 71), 0)
    return {"fields": fields, "viscous": viscous}


advect = 0.3


def compact_slope(field):
    wave = 2.0 * math.pi * jnp.arange(NX // 2 + 1, dtype=jnp.float32) / NX
    symbol = (14.0 / 9.0 * jnp.sin(wave) + jnp.sin(2.0 * wave) / 18.0) / (1.0 + 2.0 / 3.0 * jnp.cos(wave))
    spectrum = jnp.fft.rfft(field, axis=0)
    return jnp.fft.irfft(spectrum * (1j * symbol)[:, None, None], n=NX, axis=0).astype(field.dtype)


def span_slope(field):
    def shifted(offset):
        return jnp.roll(field, -offset, axis=2)
    return (45.0 * (shifted(1) - shifted(-1)) - 9.0 * (shifted(2) - shifted(-2)) + (shifted(3) - shifted(-3))) / 60.0


def wall_solve(explicit, viscous):
    diagonal = 1.0 + 2.0 * viscous
    columns = jnp.moveaxis(explicit, 1, 0)

    def forward(carry, row_values):
        previous, eliminated = carry
        current = 1.0 / (diagonal - viscous * viscous * previous)
        eliminated = current * (row_values + viscous * eliminated)
        return (current, eliminated), (current, eliminated)

    start = (jnp.zeros((), explicit.dtype), jnp.zeros_like(columns[0]))
    _, (pivots, eliminated) = lax.scan(forward, start, columns)

    def backward(solved, pair):
        pivot, value = pair
        solved = value + viscous * pivot * solved
        return solved, solved

    _, solution = lax.scan(backward, jnp.zeros_like(columns[0]), (pivots, eliminated), reverse=True)
    return jnp.moveaxis(solution, 0, 1)


def reference(fields, viscous):
    along_velocity = fields[0]
    across_velocity = fields[2]

    def one_field(pair):
        field, rate = pair
        explicit = field - advect * along_velocity * compact_slope(field) - advect * across_velocity * span_slope(field)
        return wall_solve(explicit, rate)

    return lax.map(one_field, (fields, viscous))
```

```python
import math

import jax
import jax.numpy as jnp
from jax import lax
from jax.sharding import PartitionSpec as P

advect = 0.3
root_ratio = (-1.0 + math.sqrt(5.0) / 3.0) * 1.5
line_gain = (1.0 + root_ratio * root_ratio) / (1.0 - root_ratio * root_ratio)
highest = lax.Precision.HIGHEST


def extended(array, sides, width):
    for axis, dim in sides:
        peers, length = (lax.axis_size(axis), array.shape[dim])
        up = [(i, (i + 1) % peers) for i in range(peers)]
        down = [(j, i) for i, j in up]
        last = lax.slice_in_dim(array, length - width, length, axis=dim)
        leading = lax.slice_in_dim(array, 0, width, axis=dim)
        before = lax.ppermute(last, axis, up)
        after = lax.ppermute(leading, axis, down)
        array = jnp.concatenate([before, array, after], axis=dim)
    return array


def carried_in(part, axis, combine, identity, reverse):
    count = lax.axis_size(axis)
    place = lax.axis_index(axis)
    ahead = count - 1 - place if reverse else place
    gathered = jax.tree.map(lambda a: lax.all_gather(a, axis), part)
    state = jax.tree.map(lambda a, e: jnp.zeros_like(a) + jnp.asarray(e, a.dtype), part, identity)

    def one(hop, state):
        source = count - 1 - hop if reverse else hop
        return combine(
            state, jax.tree.map(lambda a: lax.dynamic_index_in_dim(a, source, 0, False), gathered)
        )

    return lax.fori_loop(0, ahead, one, state)


def signed_power(exponent):
    parity = jnp.mod(exponent, 2.0)
    return (1.0 - 2.0 * parity) * jnp.exp(exponent * math.log(abs(root_ratio)))


def pade_kernel(length):
    row_index = jnp.arange(length, dtype=jnp.float32)[:, None]
    col_index = jnp.arange(length, dtype=jnp.float32)[None, :]
    offset = jnp.mod(row_index - col_index, float(length))
    closing = 1.0 - signed_power(jnp.float32(length))
    return line_gain * (signed_power(offset) + signed_power(length - offset)) / closing


def compact_source(line_block):

    def shifted(offset):
        return jnp.roll(line_block, -offset, axis=1)

    return 7.0 / 9.0 * (shifted(1) - shifted(-1)) + 1.0 / 36.0 * (shifted(2) - shifted(-2))


def span_derivative(fields):
    padded = extended(fields, (("gz", 3),), 3)
    span_count = fields.shape[3]

    def shifted(offset):
        return padded[..., 3 + offset : 3 + offset + span_count]

    return (
        45.0 * (shifted(1) - shifted(-1))
        - 9.0 * (shifted(2) - shifted(-2))
        + (shifted(3) - shifted(-3))
    ) / 60.0


def combine_wall(earlier, later_pair):
    return (later_pair[1][:, None, None] * earlier[0] + later_pair[0], earlier[1] * later_pair[1])


def wall_carries(explicit, viscous):
    row_count = explicit.shape[2]
    total_rows = row_count * lax.axis_size("gy")
    diagonal = 1.0 + 2.0 * viscous

    def pivot_step(previous, unused):
        current = 1.0 / (diagonal - viscous * viscous * previous)
        return (current, current)

    _, pivots = lax.scan(pivot_step, jnp.zeros_like(viscous), None, length=total_rows)
    pivots = lax.dynamic_slice_in_dim(pivots, lax.axis_index("gy") * row_count, row_count, 0).T
    log_gain = jnp.log(viscous[:, None] * pivots)
    inclusive = jnp.cumsum(log_gain, axis=1)
    exclusive = inclusive - log_gain
    row_index = jnp.arange(row_count)[:, None]
    col_index = jnp.arange(row_count)[None, :]
    lower_mask = col_index <= row_index
    upper_mask = col_index >= row_index
    spread = inclusive[:, :, None] - inclusive[:, None, :]
    forward_table = jnp.where(
        lower_mask, pivots[:, None, :] * jnp.exp(jnp.where(lower_mask, spread, 0.0)), 0.0
    )
    eliminated_local = jnp.einsum("fik,fxkz->fxiz", forward_table, explicit, precision=highest)
    block_gain = jnp.exp(inclusive[:, -1])
    zero_line = jnp.zeros_like(eliminated_local[:, :, -1])
    enter_low, _ = carried_in(
        (eliminated_local[:, :, -1], block_gain),
        "gy",
        combine_wall,
        (zero_line, jnp.ones_like(block_gain)),
        False,
    )
    eliminated = eliminated_local + jnp.exp(inclusive)[:, None, :, None] * enter_low[:, :, None, :]
    reach_log = exclusive[:, None, :] - exclusive[:, :, None]
    backward_table = jnp.where(upper_mask, jnp.exp(jnp.where(upper_mask, reach_log, 0.0)), 0.0)
    solved = jnp.einsum("fik,fxkz->fxiz", backward_table, eliminated, precision=highest)
    enter_high, _ = carried_in(
        (solved[:, :, 0], block_gain),
        "gy",
        combine_wall,
        (zero_line, jnp.ones_like(block_gain)),
        True,
    )
    trailing = jnp.exp(inclusive[:, -1:] - exclusive)
    return solved + trailing[:, None, :, None] * enter_high[:, :, None, :]


def shifted_in(array, axis, shift):
    peers = lax.axis_size(axis)
    return lax.ppermute(array, axis, [(i, (i + shift) % peers) for i in range(peers)])


def line_derivative(fields):
    peers = lax.axis_size("gx")
    length = fields.shape[1]
    total = length * peers
    padded = extended(fields, (("gx", 1),), 2)

    def plane(offset):
        return padded[:, 2 + offset : 2 + offset + length]

    source = 7.0 / 9.0 * (plane(1) - plane(-1)) + 1.0 / 36.0 * (plane(2) - plane(-2))
    index = jnp.arange(length, dtype=jnp.float32)
    distance = jnp.abs(index[:, None] - index[None, :])
    near = signed_power(distance)
    ends = jnp.stack([signed_power(length - 1 - index), signed_power(index)])
    moments = jnp.einsum("mj,fjyz->fmyz", ends, source, precision=highest)
    local = jnp.einsum("ij,fjyz->fiyz", near, source, precision=highest)
    block_weight = root_ratio**length
    left = shifted_in(moments[:, 0], "gx", 1) + block_weight * shifted_in(moments[:, 0], "gx", 2)
    right = shifted_in(moments[:, 1], "gx", -1) + block_weight * shifted_in(moments[:, 1], "gx", -2)
    span = 2
    while span < peers:
        weight = root_ratio ** (length * span)
        left = left + weight * shifted_in(left, "gx", span)
        right = right + weight * shifted_in(right, "gx", -span)
        span *= 2
    wrap = root_ratio / (1.0 - root_ratio**total)
    rising = signed_power(index)[None, :, None, None]
    falling = signed_power(length - 1 - index)[None, :, None, None]
    return line_gain * (
        local + wrap * (rising * left[:, None] + falling * right[:, None])
    )


def shards(fields, viscous):
    span_slope = span_derivative(fields)
    line_slope = line_derivative(fields)
    explicit = fields - advect * fields[0] * line_slope - advect * fields[2] * span_slope
    updated = wall_carries(explicit, viscous)
    return updated


def solution(mesh):
    in_specs = (P(None, "gx", "gy", "gz"), P())
    out_specs = P(None, "gx", "gy", "gz")
    return jax.shard_map(shards, mesh=mesh, in_specs=in_specs, out_specs=out_specs, check_vma=False)
```

```python
import math

import jax
import jax.numpy as jnp
from jax import lax
from jax.experimental import pallas as pl
from jax.sharding import PartitionSpec as P

advect = 0.3
root_ratio = (-1.0 + math.sqrt(5.0) / 3.0) * 1.5
line_gain = (1.0 + root_ratio * root_ratio) / (1.0 - root_ratio * root_ratio)
highest = lax.Precision.HIGHEST


def extended(array, sides, width):
    for axis, dim in sides:
        peers, length = (lax.axis_size(axis), array.shape[dim])
        up = [(i, (i + 1) % peers) for i in range(peers)]
        down = [(j, i) for i, j in up]
        last = lax.slice_in_dim(array, length - width, length, axis=dim)
        leading = lax.slice_in_dim(array, 0, width, axis=dim)
        before = lax.ppermute(last, axis, up)
        after = lax.ppermute(leading, axis, down)
        array = jnp.concatenate([before, array, after], axis=dim)
    return array


def signed_power(exponent):
    parity = jnp.mod(exponent, 2.0)
    return (1.0 - 2.0 * parity) * jnp.exp(exponent * math.log(abs(root_ratio)))


def span_derivative(fields):
    padded = extended(fields, (("gz", 3),), 3)
    span_count = fields.shape[3]

    def shifted(offset):
        return padded[..., 3 + offset : 3 + offset + span_count]

    return (
        45.0 * (shifted(1) - shifted(-1))
        - 9.0 * (shifted(2) - shifted(-2))
        + (shifted(3) - shifted(-3))
    ) / 60.0


def wall_pivots(viscous, total_rows):
    root = jnp.sqrt(1.0 + 4.0 * viscous)
    upper = 0.5 * (1.0 + 2.0 * viscous + root)
    log_ratio = -2.0 * jnp.log1p((1.0 + root) / (2.0 * viscous))
    rows = jnp.arange(total_rows, dtype=jnp.float32)[None, :]
    ratio_rise = jnp.expm1((rows + 1.0) * log_ratio[:, None])
    ratio_next = jnp.expm1((rows + 2.0) * log_ratio[:, None])
    return ratio_rise / (ratio_next * upper[:, None])


def carried_over(line, gains, place, count, reverse):
    step = -1 if reverse else 1
    total = jnp.zeros_like(line)
    factor = jnp.ones_like(gains[0])
    for hop in range(1, count):
        pairs = [(i, i + step * hop) for i in range(count) if 0 <= i + step * hop < count]
        arrived = lax.ppermute(line, "gy", pairs)
        total = total + factor[:, None, None] * arrived
        between = jnp.clip(place - step * hop, 0, count - 1)
        factor = factor * lax.dynamic_index_in_dim(gains, between, 0, False)
    return total


def wall_carries(explicit, viscous):
    row_count = explicit.shape[2]
    count = lax.axis_size("gy")
    place = lax.axis_index("gy")
    total_rows = row_count * count
    all_pivots = wall_pivots(viscous, total_rows)
    all_log_gain = jnp.log(viscous[:, None] * all_pivots).reshape(viscous.shape[0], count, row_count)
    gains = jnp.exp(jnp.sum(all_log_gain, axis=2)).T
    pivots = lax.dynamic_index_in_dim(all_pivots.reshape(-1, count, row_count), place, 1, False)
    log_gain = lax.dynamic_index_in_dim(all_log_gain, place, 1, False)
    inclusive = jnp.cumsum(log_gain, axis=1)
    exclusive = inclusive - log_gain
    row_index = jnp.arange(row_count)[:, None]
    col_index = jnp.arange(row_count)[None, :]
    lower_mask = col_index <= row_index
    upper_mask = col_index >= row_index
    spread = inclusive[:, :, None] - inclusive[:, None, :]
    forward_table = jnp.where(
        lower_mask, pivots[:, None, :] * jnp.exp(jnp.where(lower_mask, spread, 0.0)), 0.0
    )
    eliminated_local = jnp.einsum("fik,fxkz->fxiz", forward_table, explicit, precision=highest)
    enter_low = carried_over(eliminated_local[:, :, -1], gains, place, count, False)
    eliminated = eliminated_local + jnp.exp(inclusive)[:, None, :, None] * enter_low[:, :, None, :]
    reach_log = exclusive[:, None, :] - exclusive[:, :, None]
    backward_table = jnp.where(upper_mask, jnp.exp(jnp.where(upper_mask, reach_log, 0.0)), 0.0)
    solved = jnp.einsum("fik,fxkz->fxiz", backward_table, eliminated, precision=highest)
    enter_high = carried_over(solved[:, :, 0], gains, place, count, True)
    trailing = jnp.exp(inclusive[:, -1:] - exclusive)
    return solved + trailing[:, None, :, None] * enter_high[:, :, None, :]


def shifted_in(array, axis, shift):
    peers = lax.axis_size(axis)
    return lax.ppermute(array, axis, [(i, (i + shift) % peers) for i in range(peers)])


def line_kernel(fields_ref, before_ref, after_ref, local_ref, moments_ref):
    length = fields_ref.shape[1]

    def plane(k):
        if k < 0:
            return before_ref[0, k + 2]
        if k >= length:
            return after_ref[0, k - length]
        return fields_ref[0, k]

    def source(i):
        return 7.0 / 9.0 * (plane(i + 1) - plane(i - 1)) + 1.0 / 36.0 * (plane(i + 2) - plane(i - 2))

    running = jnp.zeros(fields_ref.shape[2:], jnp.float32)
    for i in range(length):
        running = source(i) + root_ratio * running
        local_ref[0, i] = running
    moments_ref[0, 0] = running
    running = jnp.zeros(fields_ref.shape[2:], jnp.float32)
    for i in reversed(range(length)):
        value = source(i)
        running = value + root_ratio * running
        local_ref[0, i] = line_gain * (local_ref[0, i] + running - value)
    moments_ref[0, 1] = running


def line_local(fields, before, after):
    count, length, rows, cols = fields.shape
    block = lambda depth: pl.BlockSpec((1, depth, rows, cols), lambda f: (f, 0, 0, 0))
    size = fields.size * 4
    return pl.pallas_call(
        line_kernel,
        grid=(count,),
        in_specs=[block(length), block(2), block(2)],
        out_specs=[block(length), block(2)],
        out_shape=[
            jax.ShapeDtypeStruct(fields.shape, jnp.float32),
            jax.ShapeDtypeStruct((count, 2, rows, cols), jnp.float32),
        ],
        cost_estimate=pl.CostEstimate(flops=20 * fields.size, bytes_accessed=2 * size, transcendentals=0),
    )(fields, before, after)


def line_derivative(fields):
    peers = lax.axis_size("gx")
    length = fields.shape[1]
    total = length * peers
    before = shifted_in(fields[:, length - 2 :], "gx", 1)
    after = shifted_in(fields[:, :2], "gx", -1)
    local, moments = line_local(fields, before, after)
    index = jnp.arange(length, dtype=jnp.float32)
    block_weight = root_ratio**length
    left = shifted_in(moments[:, 0], "gx", 1) + block_weight * shifted_in(moments[:, 0], "gx", 2)
    right = shifted_in(moments[:, 1], "gx", -1) + block_weight * shifted_in(moments[:, 1], "gx", -2)
    span = 2
    while span < peers:
        weight = root_ratio ** (length * span)
        left = left + weight * shifted_in(left, "gx", span)
        right = right + weight * shifted_in(right, "gx", -span)
        span *= 2
    wrap = line_gain * root_ratio / (1.0 - root_ratio**total)
    rising = signed_power(index)[None, :, None, None]
    falling = signed_power(length - 1 - index)[None, :, None, None]
    return local + wrap * (rising * left[:, None] + falling * right[:, None])


def shards(fields, viscous):
    span_slope = span_derivative(fields)
    line_slope = line_derivative(fields)
    explicit = fields - advect * fields[0] * line_slope - advect * fields[2] * span_slope
    updated = wall_carries(explicit, viscous)
    return updated


def solution(mesh):
    in_specs = (P(None, "gx", "gy", "gz"), P())
    out_specs = P(None, "gx", "gy", "gz")
    return jax.shard_map(shards, mesh=mesh, in_specs=in_specs, out_specs=out_specs, check_vma=False)
```

```python
import math

import jax
import jax.numpy as jnp
from jax import lax
from jax.experimental import pallas as pl
from jax.sharding import PartitionSpec as P

advect = 0.3
root_ratio = (-1.0 + math.sqrt(5.0) / 3.0) * 1.5
line_gain = (1.0 + root_ratio * root_ratio) / (1.0 - root_ratio * root_ratio)
highest = lax.Precision.HIGHEST


def extended(array, sides, width):
    for axis, dim in sides:
        peers, length = (lax.axis_size(axis), array.shape[dim])
        up = [(i, (i + 1) % peers) for i in range(peers)]
        down = [(j, i) for i, j in up]
        last = lax.slice_in_dim(array, length - width, length, axis=dim)
        leading = lax.slice_in_dim(array, 0, width, axis=dim)
        before = lax.ppermute(last, axis, up)
        after = lax.ppermute(leading, axis, down)
        array = jnp.concatenate([before, array, after], axis=dim)
    return array


def signed_power(exponent):
    parity = jnp.mod(exponent, 2.0)
    return (1.0 - 2.0 * parity) * jnp.exp(exponent * math.log(abs(root_ratio)))


def span_derivative(fields):
    padded = extended(fields, (("gz", 3),), 3)
    span_count = fields.shape[3]

    def shifted(offset):
        return padded[..., 3 + offset : 3 + offset + span_count]

    return (
        45.0 * (shifted(1) - shifted(-1))
        - 9.0 * (shifted(2) - shifted(-2))
        + (shifted(3) - shifted(-3))
    ) / 60.0


def wall_pivots(viscous, total_rows):
    root = jnp.sqrt(1.0 + 4.0 * viscous)
    upper = 0.5 * (1.0 + 2.0 * viscous + root)
    log_ratio = -2.0 * jnp.log1p((1.0 + root) / (2.0 * viscous))
    rows = jnp.arange(total_rows, dtype=jnp.float32)[None, :]
    ratio_rise = jnp.expm1((rows + 1.0) * log_ratio[:, None])
    ratio_next = jnp.expm1((rows + 2.0) * log_ratio[:, None])
    return ratio_rise / (ratio_next * upper[:, None])


def carried_over(line, gains, place, count, reverse):
    step = -1 if reverse else 1
    total = jnp.zeros_like(line)
    factor = jnp.ones_like(gains[0])
    for hop in range(1, count):
        pairs = [(i, i + step * hop) for i in range(count) if 0 <= i + step * hop < count]
        arrived = lax.ppermute(line, "gy", pairs)
        total = total + factor[:, None, None] * arrived
        between = jnp.clip(place - step * hop, 0, count - 1)
        factor = factor * lax.dynamic_index_in_dim(gains, between, 0, False)
    return total


def wall_carries(explicit, viscous):
    row_count = explicit.shape[2]
    count = lax.axis_size("gy")
    place = lax.axis_index("gy")
    total_rows = row_count * count
    all_pivots = wall_pivots(viscous, total_rows)
    all_log_gain = jnp.log(viscous[:, None] * all_pivots).reshape(viscous.shape[0], count, row_count)
    gains = jnp.exp(jnp.sum(all_log_gain, axis=2)).T
    pivots = lax.dynamic_index_in_dim(all_pivots.reshape(-1, count, row_count), place, 1, False)
    log_gain = lax.dynamic_index_in_dim(all_log_gain, place, 1, False)
    inclusive = jnp.cumsum(log_gain, axis=1)
    exclusive = inclusive - log_gain
    row_index = jnp.arange(row_count)[:, None]
    col_index = jnp.arange(row_count)[None, :]
    lower_mask = col_index <= row_index
    upper_mask = col_index >= row_index
    spread = inclusive[:, :, None] - inclusive[:, None, :]
    forward_table = jnp.where(
        lower_mask, pivots[:, None, :] * jnp.exp(jnp.where(lower_mask, spread, 0.0)), 0.0
    )
    eliminated_local = jnp.einsum("fik,fxkz->fxiz", forward_table, explicit, precision=highest)
    enter_low = carried_over(eliminated_local[:, :, -1], gains, place, count, False)
    eliminated = eliminated_local + jnp.exp(inclusive)[:, None, :, None] * enter_low[:, :, None, :]
    reach_log = exclusive[:, None, :] - exclusive[:, :, None]
    backward_table = jnp.where(upper_mask, jnp.exp(jnp.where(upper_mask, reach_log, 0.0)), 0.0)
    solved = jnp.einsum("fik,fxkz->fxiz", backward_table, eliminated, precision=highest)
    enter_high = carried_over(solved[:, :, 0], gains, place, count, True)
    trailing = jnp.exp(inclusive[:, -1:] - exclusive)
    return solved + trailing[:, None, :, None] * enter_high[:, :, None, :]


def shifted_in(array, axis, shift):
    peers = lax.axis_size(axis)
    return lax.ppermute(array, axis, [(i, (i + shift) % peers) for i in range(peers)])


def line_kernel(fields_ref, before_ref, after_ref, local_ref, moments_ref):
    length = fields_ref.shape[1]

    def plane(k):
        if k < 0:
            return before_ref[0, k + 2]
        if k >= length:
            return after_ref[0, k - length]
        return fields_ref[0, k]

    def source(i):
        return 7.0 / 9.0 * (plane(i + 1) - plane(i - 1)) + 1.0 / 36.0 * (plane(i + 2) - plane(i - 2))

    running = jnp.zeros(fields_ref.shape[2:], jnp.float32)
    for i in range(length):
        running = source(i) + root_ratio * running
        local_ref[0, i] = running
    moments_ref[0, 0] = running
    running = jnp.zeros(fields_ref.shape[2:], jnp.float32)
    for i in reversed(range(length)):
        value = source(i)
        running = value + root_ratio * running
        local_ref[0, i] = line_gain * (local_ref[0, i] + running - value)
    moments_ref[0, 1] = running


def line_local(fields, before, after):
    count, length, rows, cols = fields.shape
    block = lambda depth: pl.BlockSpec((1, depth, rows, cols), lambda f: (f, 0, 0, 0))
    size = fields.size * 4
    return pl.pallas_call(
        line_kernel,
        grid=(count,),
        in_specs=[block(length), block(2), block(2)],
        out_specs=[block(length), block(2)],
        out_shape=[
            jax.ShapeDtypeStruct(fields.shape, jnp.float32),
            jax.ShapeDtypeStruct((count, 2, rows, cols), jnp.float32),
        ],
        cost_estimate=pl.CostEstimate(flops=20 * fields.size, bytes_accessed=2 * size, transcendentals=0),
    )(fields, before, after)


def line_carries(moments, length):
    peers = lax.axis_size("gx")
    block_weight = root_ratio**length
    left = shifted_in(moments[:, 0], "gx", 1) + block_weight * shifted_in(moments[:, 0], "gx", 2)
    right = shifted_in(moments[:, 1], "gx", -1) + block_weight * shifted_in(moments[:, 1], "gx", -2)
    span = 2
    while span < peers:
        weight = root_ratio ** (length * span)
        left = left + weight * shifted_in(left, "gx", span)
        right = right + weight * shifted_in(right, "gx", -span)
        span *= 2
    return left, right


def shards(fields, viscous):
    length = fields.shape[1]
    total = length * lax.axis_size("gx")
    before = shifted_in(fields[:, length - 2 :], "gx", 1)
    after = shifted_in(fields[:, :2], "gx", -1)
    local, moments = line_local(fields, before, after)
    late_fields, local = lax.optimization_barrier((fields, local))
    span_slope = span_derivative(late_fields)
    partial = late_fields - advect * late_fields[0] * local - advect * late_fields[2] * span_slope
    left, right = line_carries(moments, length)
    partial, left, right = lax.optimization_barrier((partial, left, right))
    index = jnp.arange(length, dtype=jnp.float32)
    wrap = line_gain * root_ratio / (1.0 - root_ratio**total)
    rising = signed_power(index)[None, :, None, None]
    falling = signed_power(length - 1 - index)[None, :, None, None]
    carried = wrap * (rising * left[:, None] + falling * right[:, None])
    explicit = partial - advect * fields[0] * carried
    updated = wall_carries(explicit, viscous)
    return updated


def solution(mesh):
    in_specs = (P(None, "gx", "gy", "gz"), P())
    out_specs = P(None, "gx", "gy", "gz")
    return jax.shard_map(shards, mesh=mesh, in_specs=in_specs, out_specs=out_specs, check_vma=False)
```

```python
import math

import jax
import jax.numpy as jnp
from jax import lax
from jax.experimental import pallas as pl
from jax.sharding import PartitionSpec as P

advect = 0.3
root_ratio = (-1.0 + math.sqrt(5.0) / 3.0) * 1.5
line_gain = (1.0 + root_ratio * root_ratio) / (1.0 - root_ratio * root_ratio)
highest = lax.Precision.HIGHEST


def signed_power(exponent):
    parity = jnp.mod(exponent, 2.0)
    return (1.0 - 2.0 * parity) * jnp.exp(exponent * math.log(abs(root_ratio)))


def span_weights(offset):
    weights = {1: 45.0, -1: -45.0, 2: -9.0, -2: 9.0, 3: 1.0, -3: -1.0}
    return sum((w / 60.0) * (offset == k).astype(jnp.float32) for k, w in weights.items())


def span_derivative(fields):
    cols = fields.shape[3]
    lanes = jnp.arange(cols)
    halo = jnp.arange(3)
    interior = span_weights(lanes[:, None] - lanes[None, :])
    pick = jnp.concatenate(
        [lanes[None, :] == cols - 3 + halo[:, None], lanes[None, :] == halo[:, None]]
    ).astype(jnp.float32)
    edges = jnp.einsum("cz,fxyz->fxcy", pick, fields, precision=highest)
    before = shifted_in(edges[:, :, :3], "gz", 1)
    after = shifted_in(edges[:, :, 3:], "gz", -1)
    before_weights = span_weights(halo[:, None] - 3 - lanes[None, :])
    after_weights = span_weights(halo[:, None] + cols - lanes[None, :])
    return (
        jnp.einsum("fxyw,wz->fxyz", fields, interior, precision=highest)
        + jnp.einsum("fxcy,cz->fxyz", before, before_weights, precision=highest)
        + jnp.einsum("fxcy,cz->fxyz", after, after_weights, precision=highest)
    )


def wall_pivots(viscous, total_rows):
    root = jnp.sqrt(1.0 + 4.0 * viscous)
    upper = 0.5 * (1.0 + 2.0 * viscous + root)
    log_ratio = -2.0 * jnp.log1p((1.0 + root) / (2.0 * viscous))
    rows = jnp.arange(total_rows, dtype=jnp.float32)[None, :]
    ratio_rise = jnp.expm1((rows + 1.0) * log_ratio[:, None])
    ratio_next = jnp.expm1((rows + 2.0) * log_ratio[:, None])
    return ratio_rise / (ratio_next * upper[:, None])


def carried_over(line, gains, place, count, reverse):
    step = -1 if reverse else 1
    total = jnp.zeros_like(line)
    factor = jnp.ones_like(gains[0])
    for hop in range(1, count):
        pairs = [(i, i + step * hop) for i in range(count) if 0 <= i + step * hop < count]
        arrived = lax.ppermute(line, "gy", pairs)
        total = total + factor[:, None, None] * arrived
        between = jnp.clip(place - step * hop, 0, count - 1)
        factor = factor * lax.dynamic_index_in_dim(gains, between, 0, False)
    return total


def wall_carries(explicit, viscous):
    row_count = explicit.shape[2]
    count = lax.axis_size("gy")
    place = lax.axis_index("gy")
    total_rows = row_count * count
    all_pivots = wall_pivots(viscous, total_rows)
    all_log_gain = jnp.log(viscous[:, None] * all_pivots).reshape(viscous.shape[0], count, row_count)
    gains = jnp.exp(jnp.sum(all_log_gain, axis=2)).T
    pivots = lax.dynamic_index_in_dim(all_pivots.reshape(-1, count, row_count), place, 1, False)
    log_gain = lax.dynamic_index_in_dim(all_log_gain, place, 1, False)
    inclusive = jnp.cumsum(log_gain, axis=1)
    exclusive = inclusive - log_gain
    row_index = jnp.arange(row_count)[:, None]
    col_index = jnp.arange(row_count)[None, :]
    lower_mask = col_index <= row_index
    upper_mask = col_index >= row_index
    spread = inclusive[:, :, None] - inclusive[:, None, :]
    forward_table = jnp.where(
        lower_mask, pivots[:, None, :] * jnp.exp(jnp.where(lower_mask, spread, 0.0)), 0.0
    )
    eliminated_local = jnp.einsum("fik,fxkz->fxiz", forward_table, explicit, precision=highest)
    enter_low = carried_over(eliminated_local[:, :, -1], gains, place, count, False)
    eliminated = eliminated_local + jnp.exp(inclusive)[:, None, :, None] * enter_low[:, :, None, :]
    reach_log = exclusive[:, None, :] - exclusive[:, :, None]
    backward_table = jnp.where(upper_mask, jnp.exp(jnp.where(upper_mask, reach_log, 0.0)), 0.0)
    solved = jnp.einsum("fik,fxkz->fxiz", backward_table, eliminated, precision=highest)
    enter_high = carried_over(solved[:, :, 0], gains, place, count, True)
    trailing = jnp.exp(inclusive[:, -1:] - exclusive)
    return solved + trailing[:, None, :, None] * enter_high[:, :, None, :]


def shifted_in(array, axis, shift):
    peers = lax.axis_size(axis)
    return lax.ppermute(array, axis, [(i, (i + shift) % peers) for i in range(peers)])


def line_kernel(fields_ref, before_ref, after_ref, local_ref, moments_ref):
    length = fields_ref.shape[1]

    def plane(k):
        if k < 0:
            return before_ref[0, k + 2]
        if k >= length:
            return after_ref[0, k - length]
        return fields_ref[0, k]

    def source(i):
        return 7.0 / 9.0 * (plane(i + 1) - plane(i - 1)) + 1.0 / 36.0 * (plane(i + 2) - plane(i - 2))

    running = jnp.zeros(fields_ref.shape[2:], jnp.float32)
    for i in range(length):
        running = source(i) + root_ratio * running
        local_ref[0, i] = running
    moments_ref[0, 0] = running
    running = jnp.zeros(fields_ref.shape[2:], jnp.float32)
    for i in reversed(range(length)):
        value = source(i)
        running = value + root_ratio * running
        local_ref[0, i] = line_gain * (local_ref[0, i] + running - value)
    moments_ref[0, 1] = running


def line_local(fields, before, after):
    count, length, rows, cols = fields.shape
    block = lambda depth: pl.BlockSpec((1, depth, rows, cols), lambda f: (f, 0, 0, 0))
    size = fields.size * 4
    return pl.pallas_call(
        line_kernel,
        grid=(count,),
        in_specs=[block(length), block(2), block(2)],
        out_specs=[block(length), block(2)],
        out_shape=[
            jax.ShapeDtypeStruct(fields.shape, jnp.float32),
            jax.ShapeDtypeStruct((count, 2, rows, cols), jnp.float32),
        ],
        cost_estimate=pl.CostEstimate(flops=20 * fields.size, bytes_accessed=2 * size, transcendentals=0),
    )(fields, before, after)


def line_carries(moments, length):
    peers = lax.axis_size("gx")
    block_weight = root_ratio**length
    left = shifted_in(moments[:, 0], "gx", 1) + block_weight * shifted_in(moments[:, 0], "gx", 2)
    right = shifted_in(moments[:, 1], "gx", -1) + block_weight * shifted_in(moments[:, 1], "gx", -2)
    span = 2
    while span < peers:
        weight = root_ratio ** (length * span)
        left = left + weight * shifted_in(left, "gx", span)
        right = right + weight * shifted_in(right, "gx", -span)
        span *= 2
    return left, right


def shards(fields, viscous):
    length = fields.shape[1]
    total = length * lax.axis_size("gx")
    before = shifted_in(fields[:, length - 2 :], "gx", 1)
    after = shifted_in(fields[:, :2], "gx", -1)
    local, moments = line_local(fields, before, after)
    late_fields, local = lax.optimization_barrier((fields, local))
    span_slope = span_derivative(late_fields)
    partial = late_fields - advect * late_fields[0] * local - advect * late_fields[2] * span_slope
    left, right = line_carries(moments, length)
    partial, left, right = lax.optimization_barrier((partial, left, right))
    index = jnp.arange(length, dtype=jnp.float32)
    wrap = line_gain * root_ratio / (1.0 - root_ratio**total)
    rising = signed_power(index)[None, :, None, None]
    falling = signed_power(length - 1 - index)[None, :, None, None]
    carried = wrap * (rising * left[:, None] + falling * right[:, None])
    explicit = partial - advect * fields[0] * carried
    updated = wall_carries(explicit, viscous)
    return updated


def solution(mesh):
    in_specs = (P(None, "gx", "gy", "gz"), P())
    out_specs = P(None, "gx", "gy", "gz")
    return jax.shard_map(shards, mesh=mesh, in_specs=in_specs, out_specs=out_specs, check_vma=False)
```

```python
import math

import jax
import jax.numpy as jnp
from jax import lax
from jax.experimental import pallas as pl
from jax.sharding import PartitionSpec as P

advect = 0.3
root_ratio = (-1.0 + math.sqrt(5.0) / 3.0) * 1.5
line_gain = (1.0 + root_ratio * root_ratio) / (1.0 - root_ratio * root_ratio)
highest = lax.Precision.HIGHEST


def signed_power(exponent):
    parity = jnp.mod(exponent, 2.0)
    return (1.0 - 2.0 * parity) * jnp.exp(exponent * math.log(abs(root_ratio)))


def span_weights(offset):
    weights = {1: 45.0, -1: -45.0, 2: -9.0, -2: 9.0, 3: 1.0, -3: -1.0}
    return sum((w / 60.0) * (offset == k).astype(jnp.float32) for k, w in weights.items())


def span_halos(fields):
    cols = fields.shape[3]
    lanes = jnp.arange(cols)
    halo = jnp.arange(3)
    pick = jnp.concatenate(
        [lanes[None, :] == cols - 3 + halo[:, None], lanes[None, :] == halo[:, None]]
    ).astype(jnp.float32)
    edges = jnp.einsum("cz,fxyz->fxcy", pick, fields, precision=highest)
    return shifted_in(edges[:, :, :3], "gz", 1), shifted_in(edges[:, :, 3:], "gz", -1)


def span_inner(fields):
    lanes = jnp.arange(fields.shape[3])
    interior = span_weights(lanes[:, None] - lanes[None, :])
    return jnp.einsum("fxyw,wz->fxyz", fields, interior, precision=highest)


def span_finish(inner, before, after):
    cols = inner.shape[3]
    lanes = jnp.arange(cols)
    halo = jnp.arange(3)
    before_weights = span_weights(halo[:, None] - 3 - lanes[None, :])
    after_weights = span_weights(halo[:, None] + cols - lanes[None, :])
    return (
        inner
        + jnp.einsum("fxcy,cz->fxyz", before, before_weights, precision=highest)
        + jnp.einsum("fxcy,cz->fxyz", after, after_weights, precision=highest)
    )


def wall_pivots(viscous, total_rows):
    root = jnp.sqrt(1.0 + 4.0 * viscous)
    upper = 0.5 * (1.0 + 2.0 * viscous + root)
    log_ratio = -2.0 * jnp.log1p((1.0 + root) / (2.0 * viscous))
    rows = jnp.arange(total_rows, dtype=jnp.float32)[None, :]
    ratio_rise = jnp.expm1((rows + 1.0) * log_ratio[:, None])
    ratio_next = jnp.expm1((rows + 2.0) * log_ratio[:, None])
    return ratio_rise / (ratio_next * upper[:, None])


def carried_over(line, gains, place, count, reverse):
    step = -1 if reverse else 1
    total = jnp.zeros_like(line)
    factor = jnp.ones_like(gains[0])
    for hop in range(1, count):
        pairs = [(i, i + step * hop) for i in range(count) if 0 <= i + step * hop < count]
        arrived = lax.ppermute(line, "gy", pairs)
        total = total + factor[:, None, None] * arrived
        between = jnp.clip(place - step * hop, 0, count - 1)
        factor = factor * lax.dynamic_index_in_dim(gains, between, 0, False)
    return total


def wall_carries(explicit, viscous):
    row_count = explicit.shape[2]
    count = lax.axis_size("gy")
    place = lax.axis_index("gy")
    total_rows = row_count * count
    all_pivots = wall_pivots(viscous, total_rows)
    all_log_gain = jnp.log(viscous[:, None] * all_pivots).reshape(viscous.shape[0], count, row_count)
    gains = jnp.exp(jnp.sum(all_log_gain, axis=2)).T
    pivots = lax.dynamic_index_in_dim(all_pivots.reshape(-1, count, row_count), place, 1, False)
    log_gain = lax.dynamic_index_in_dim(all_log_gain, place, 1, False)
    inclusive = jnp.cumsum(log_gain, axis=1)
    exclusive = inclusive - log_gain
    row_index = jnp.arange(row_count)[:, None]
    col_index = jnp.arange(row_count)[None, :]
    lower_mask = col_index <= row_index
    upper_mask = col_index >= row_index
    spread = inclusive[:, :, None] - inclusive[:, None, :]
    forward_table = jnp.where(
        lower_mask, pivots[:, None, :] * jnp.exp(jnp.where(lower_mask, spread, 0.0)), 0.0
    )
    eliminated_local = jnp.einsum("fik,fxkz->fxiz", forward_table, explicit, precision=highest)
    enter_low = carried_over(eliminated_local[:, :, -1], gains, place, count, False)
    eliminated = eliminated_local + jnp.exp(inclusive)[:, None, :, None] * enter_low[:, :, None, :]
    reach_log = exclusive[:, None, :] - exclusive[:, :, None]
    backward_table = jnp.where(upper_mask, jnp.exp(jnp.where(upper_mask, reach_log, 0.0)), 0.0)
    solved = jnp.einsum("fik,fxkz->fxiz", backward_table, eliminated, precision=highest)
    enter_high = carried_over(solved[:, :, 0], gains, place, count, True)
    trailing = jnp.exp(inclusive[:, -1:] - exclusive)
    return solved + trailing[:, None, :, None] * enter_high[:, :, None, :]


def shifted_in(array, axis, shift):
    peers = lax.axis_size(axis)
    return lax.ppermute(array, axis, [(i, (i + shift) % peers) for i in range(peers)])


def line_kernel(fields_ref, before_ref, after_ref, local_ref, moments_ref):
    length = fields_ref.shape[1]

    def plane(k):
        if k < 0:
            return before_ref[0, k + 2]
        if k >= length:
            return after_ref[0, k - length]
        return fields_ref[0, k]

    def source(i):
        return 7.0 / 9.0 * (plane(i + 1) - plane(i - 1)) + 1.0 / 36.0 * (plane(i + 2) - plane(i - 2))

    running = jnp.zeros(fields_ref.shape[2:], jnp.float32)
    for i in range(length):
        running = source(i) + root_ratio * running
        local_ref[0, i] = running
    moments_ref[0, 0] = running
    running = jnp.zeros(fields_ref.shape[2:], jnp.float32)
    for i in reversed(range(length)):
        value = source(i)
        running = value + root_ratio * running
        local_ref[0, i] = line_gain * (local_ref[0, i] + running - value)
    moments_ref[0, 1] = running


def line_local(fields, before, after):
    count, length, rows, cols = fields.shape
    block = lambda depth: pl.BlockSpec((1, depth, rows, cols), lambda f: (f, 0, 0, 0))
    size = fields.size * 4
    return pl.pallas_call(
        line_kernel,
        grid=(count,),
        in_specs=[block(length), block(2), block(2)],
        out_specs=[block(length), block(2)],
        out_shape=[
            jax.ShapeDtypeStruct(fields.shape, jnp.float32),
            jax.ShapeDtypeStruct((count, 2, rows, cols), jnp.float32),
        ],
        cost_estimate=pl.CostEstimate(flops=20 * fields.size, bytes_accessed=2 * size, transcendentals=0),
    )(fields, before, after)


def shards(fields, viscous):
    length = fields.shape[1]
    peers = lax.axis_size("gx")
    total = length * peers
    before = shifted_in(fields[:, length - 2 :], "gx", 1)
    after = shifted_in(fields[:, :2], "gx", -1)
    local, moments = line_local(fields, before, after)
    late, local, moments = lax.optimization_barrier((fields, local, moments))
    block_weight = root_ratio**length
    arrived = (
        shifted_in(moments[:, 0], "gx", 1),
        shifted_in(moments[:, 0], "gx", 2),
        shifted_in(moments[:, 1], "gx", -1),
        shifted_in(moments[:, 1], "gx", -2),
    )
    state = {"inner": span_inner(late), "halos": span_halos(late)}
    state, arrived = lax.optimization_barrier((state, arrived))
    left = arrived[0] + block_weight * arrived[1]
    right = arrived[2] + block_weight * arrived[3]
    spans = []
    span = 2
    while span < peers:
        spans.append(span)
        span *= 2

    def finish_span(state):
        state["span"] = span_finish(state["inner"], *state["halos"])

    def finish_partial(state):
        state["partial"] = late - advect * late[0] * local - advect * late[2] * state["span"]

    if not spans:
        finish_span(state)
        finish_partial(state)
    for step, span in enumerate(spans):
        state, left, right = lax.optimization_barrier((state, left, right))
        from_left = shifted_in(left, "gx", span)
        from_right = shifted_in(right, "gx", -span)
        if step == 0:
            finish_span(state)
        if step == len(spans) - 1:
            finish_partial(state)
        state, from_left, from_right = lax.optimization_barrier((state, from_left, from_right))
        weight = root_ratio ** (length * span)
        left = left + weight * from_left
        right = right + weight * from_right
    index = jnp.arange(length, dtype=jnp.float32)
    wrap = line_gain * root_ratio / (1.0 - root_ratio**total)
    rising = signed_power(index)[None, :, None, None]
    falling = signed_power(length - 1 - index)[None, :, None, None]
    carried = wrap * (rising * left[:, None] + falling * right[:, None])
    explicit = state["partial"] - advect * fields[0] * carried
    updated = wall_carries(explicit, viscous)
    return updated


def solution(mesh):
    in_specs = (P(None, "gx", "gy", "gz"), P())
    out_specs = P(None, "gx", "gy", "gz")
    return jax.shard_map(shards, mesh=mesh, in_specs=in_specs, out_specs=out_specs, check_vma=False)
```

```python
import math

import jax
import jax.numpy as jnp
from jax import lax
from jax.experimental import pallas as pl
from jax.sharding import PartitionSpec as P

advect = 0.3
root_ratio = (-1.0 + math.sqrt(5.0) / 3.0) * 1.5
line_gain = (1.0 + root_ratio * root_ratio) / (1.0 - root_ratio * root_ratio)
highest = lax.Precision.HIGHEST


def signed_power(exponent):
    parity = jnp.mod(exponent, 2.0)
    return (1.0 - 2.0 * parity) * jnp.exp(exponent * math.log(abs(root_ratio)))


def span_weights(offset):
    weights = {1: 45.0, -1: -45.0, 2: -9.0, -2: 9.0, 3: 1.0, -3: -1.0}
    return sum((w / 60.0) * (offset == k).astype(jnp.float32) for k, w in weights.items())


def span_halos(fields):
    cols = fields.shape[3]
    lanes = jnp.arange(cols)
    halo = jnp.arange(3)
    pick = jnp.concatenate(
        [lanes[None, :] == cols - 3 + halo[:, None], lanes[None, :] == halo[:, None]]
    ).astype(jnp.float32)
    edges = jnp.einsum("cz,fxyz->fxcy", pick, fields, precision=highest)
    return shifted_in(edges[:, :, :3], "gz", 1), shifted_in(edges[:, :, 3:], "gz", -1)


def span_inner(fields):
    lanes = jnp.arange(fields.shape[3])
    interior = span_weights(lanes[:, None] - lanes[None, :])
    return jnp.einsum("fxyw,wz->fxyz", fields, interior, precision=highest)


def span_halo_term(before, after, cols):
    lanes = jnp.arange(cols)
    halo = jnp.arange(3)
    weights = jnp.concatenate(
        [span_weights(halo[:, None] - 3 - lanes[None, :]), span_weights(halo[:, None] + cols - lanes[None, :])]
    )
    stacked = jnp.concatenate([before, after], axis=2)
    return jnp.einsum("fxcy,cz->fxyz", stacked, weights, precision=highest)

def wall_pivots(viscous, total_rows):
    root = jnp.sqrt(1.0 + 4.0 * viscous)
    upper = 0.5 * (1.0 + 2.0 * viscous + root)
    log_ratio = -2.0 * jnp.log1p((1.0 + root) / (2.0 * viscous))
    rows = jnp.arange(total_rows, dtype=jnp.float32)[None, :]
    ratio_rise = jnp.expm1((rows + 1.0) * log_ratio[:, None])
    ratio_next = jnp.expm1((rows + 2.0) * log_ratio[:, None])
    return ratio_rise / (ratio_next * upper[:, None])


def carried_over(line, gains, place, count, reverse):
    step = -1 if reverse else 1
    total = jnp.zeros_like(line)
    factor = jnp.ones_like(gains[0])
    for hop in range(1, count):
        pairs = [(i, i + step * hop) for i in range(count) if 0 <= i + step * hop < count]
        arrived = lax.ppermute(line, "gy", pairs)
        total = total + factor[:, None, None] * arrived
        between = jnp.clip(place - step * hop, 0, count - 1)
        factor = factor * lax.dynamic_index_in_dim(gains, between, 0, False)
    return total


def wall_carries(explicit, viscous):
    row_count = explicit.shape[2]
    count = lax.axis_size("gy")
    place = lax.axis_index("gy")
    total_rows = row_count * count
    all_pivots = wall_pivots(viscous, total_rows)
    all_log_gain = jnp.log(viscous[:, None] * all_pivots).reshape(viscous.shape[0], count, row_count)
    gains = jnp.exp(jnp.sum(all_log_gain, axis=2)).T
    pivots = lax.dynamic_index_in_dim(all_pivots.reshape(-1, count, row_count), place, 1, False)
    log_gain = lax.dynamic_index_in_dim(all_log_gain, place, 1, False)
    inclusive = jnp.cumsum(log_gain, axis=1)
    exclusive = inclusive - log_gain
    row_index = jnp.arange(row_count)[:, None]
    col_index = jnp.arange(row_count)[None, :]
    lower_mask = col_index <= row_index
    upper_mask = col_index >= row_index
    spread = inclusive[:, :, None] - inclusive[:, None, :]
    forward_table = jnp.where(
        lower_mask, pivots[:, None, :] * jnp.exp(jnp.where(lower_mask, spread, 0.0)), 0.0
    )
    eliminated_local = jnp.einsum("fik,fxkz->fxiz", forward_table, explicit, precision=highest)
    enter_low = carried_over(eliminated_local[:, :, -1], gains, place, count, False)
    eliminated = eliminated_local + jnp.exp(inclusive)[:, None, :, None] * enter_low[:, :, None, :]
    reach_log = exclusive[:, None, :] - exclusive[:, :, None]
    backward_table = jnp.where(upper_mask, jnp.exp(jnp.where(upper_mask, reach_log, 0.0)), 0.0)
    solved = jnp.einsum("fik,fxkz->fxiz", backward_table, eliminated, precision=highest)
    enter_high = carried_over(solved[:, :, 0], gains, place, count, True)
    trailing = jnp.exp(inclusive[:, -1:] - exclusive)
    return solved + trailing[:, None, :, None] * enter_high[:, :, None, :]


def shifted_in(array, axis, shift):
    peers = lax.axis_size(axis)
    return lax.ppermute(array, axis, [(i, (i + shift) % peers) for i in range(peers)])


def line_kernel(fields_ref, before_ref, after_ref, local_ref, moments_ref):
    length = fields_ref.shape[1]

    def plane(k):
        if k < 0:
            return before_ref[0, k + 2]
        if k >= length:
            return after_ref[0, k - length]
        return fields_ref[0, k]

    def source(i):
        return 7.0 / 9.0 * (plane(i + 1) - plane(i - 1)) + 1.0 / 36.0 * (plane(i + 2) - plane(i - 2))

    running = jnp.zeros(fields_ref.shape[2:], jnp.float32)
    for i in range(length):
        running = source(i) + root_ratio * running
        local_ref[0, i] = running
    moments_ref[0, 0] = running
    running = jnp.zeros(fields_ref.shape[2:], jnp.float32)
    for i in reversed(range(length)):
        value = source(i)
        running = value + root_ratio * running
        local_ref[0, i] = line_gain * (local_ref[0, i] + running - value)
    moments_ref[0, 1] = running


def line_local(fields, before, after):
    count, length, rows, cols = fields.shape
    block = lambda depth: pl.BlockSpec((1, depth, rows, cols), lambda f: (f, 0, 0, 0))
    size = fields.size * 4
    return pl.pallas_call(
        line_kernel,
        grid=(count,),
        in_specs=[block(length), block(2), block(2)],
        out_specs=[block(length), block(2)],
        out_shape=[
            jax.ShapeDtypeStruct(fields.shape, jnp.float32),
            jax.ShapeDtypeStruct((count, 2, rows, cols), jnp.float32),
        ],
        cost_estimate=pl.CostEstimate(flops=20 * fields.size, bytes_accessed=2 * size, transcendentals=0),
    )(fields, before, after)


def shards(fields, viscous):
    length = fields.shape[1]
    peers = lax.axis_size("gx")
    total = length * peers
    before = shifted_in(fields[:, length - 2 :], "gx", 1)
    after = shifted_in(fields[:, :2], "gx", -1)
    local, moments = line_local(fields, before, after)
    late, local, moments = lax.optimization_barrier((fields, local, moments))
    block_weight = root_ratio**length
    arrived = (
        shifted_in(moments[:, 0], "gx", 1),
        shifted_in(moments[:, 0], "gx", 2),
        shifted_in(moments[:, 1], "gx", -1),
        shifted_in(moments[:, 1], "gx", -2),
    )
    state = {"halos": span_halos(late)}
    state, arrived = lax.optimization_barrier((state, arrived))
    left = arrived[0] + block_weight * arrived[1]
    right = arrived[2] + block_weight * arrived[3]
    spans = []
    span = 2
    while span < peers:
        spans.append(span)
        span *= 2

    def inner_part(state):
        inner = span_inner(late)
        state["partial"] = late - advect * late[0] * local - advect * late[2] * inner

    def halo_part(state):
        halo_term = span_halo_term(*state["halos"], late.shape[3])
        state["partial"] = state["partial"] - advect * late[2] * halo_term

    tasks = [inner_part, halo_part]
    for span in spans:
        state, left, right = lax.optimization_barrier((state, left, right))
        from_left = shifted_in(left, "gx", span)
        from_right = shifted_in(right, "gx", -span)
        if tasks and span != spans[-1]:
            tasks.pop(0)(state)
        elif span == spans[-1]:
            while tasks:
                tasks.pop(0)(state)
        state, from_left, from_right = lax.optimization_barrier((state, from_left, from_right))
        weight = root_ratio ** (length * span)
        left = left + weight * from_left
        right = right + weight * from_right
    while tasks:
        tasks.pop(0)(state)
    index = jnp.arange(length, dtype=jnp.float32)
    wrap = line_gain * root_ratio / (1.0 - root_ratio**total)
    rising = signed_power(index)[None, :, None, None]
    falling = signed_power(length - 1 - index)[None, :, None, None]
    carried = wrap * (rising * left[:, None] + falling * right[:, None])
    explicit = state["partial"] - advect * fields[0] * carried
    updated = wall_carries(explicit, viscous)
    return updated


def solution(mesh):
    in_specs = (P(None, "gx", "gy", "gz"), P())
    out_specs = P(None, "gx", "gy", "gz")
    return jax.shard_map(shards, mesh=mesh, in_specs=in_specs, out_specs=out_specs, check_vma=False)
```

```python
import math

import jax
import jax.numpy as jnp
from jax import lax
from jax.experimental import pallas as pl
from jax.sharding import PartitionSpec as P

advect = 0.3
root_ratio = (-1.0 + math.sqrt(5.0) / 3.0) * 1.5
line_gain = (1.0 + root_ratio * root_ratio) / (1.0 - root_ratio * root_ratio)
highest = lax.Precision.HIGHEST


def signed_power(exponent):
    parity = jnp.mod(exponent, 2.0)
    return (1.0 - 2.0 * parity) * jnp.exp(exponent * math.log(abs(root_ratio)))


def span_weights(offset):
    weights = {1: 45.0, -1: -45.0, 2: -9.0, -2: 9.0, 3: 1.0, -3: -1.0}
    return sum((w / 60.0) * (offset == k).astype(jnp.float32) for k, w in weights.items())


def span_halos(fields):
    cols = fields.shape[3]
    lanes = jnp.arange(cols)
    halo = jnp.arange(3)
    pick = jnp.concatenate(
        [lanes[None, :] == cols - 3 + halo[:, None], lanes[None, :] == halo[:, None]]
    ).astype(jnp.float32)
    edges = jnp.einsum("cz,fxyz->fxcy", pick, fields, precision=highest)
    return shifted_in(edges[:, :, :3], "gz", 1), shifted_in(edges[:, :, 3:], "gz", -1)


def span_inner(fields):
    lanes = jnp.arange(fields.shape[3])
    interior = span_weights(lanes[:, None] - lanes[None, :])
    return jnp.einsum("fxyw,wz->fxyz", fields, interior, precision=highest)


def span_halo_term(before, after, cols):
    lanes = jnp.arange(cols)
    halo = jnp.arange(3)
    weights = jnp.concatenate(
        [span_weights(halo[:, None] - 3 - lanes[None, :]), span_weights(halo[:, None] + cols - lanes[None, :])]
    )
    stacked = jnp.concatenate([before, after], axis=2)
    return jnp.einsum("fxcy,cz->fxyz", stacked, weights, precision=highest)

def wall_pivots(viscous, total_rows):
    root = jnp.sqrt(1.0 + 4.0 * viscous)
    upper = 0.5 * (1.0 + 2.0 * viscous + root)
    log_ratio = -2.0 * jnp.log1p((1.0 + root) / (2.0 * viscous))
    rows = jnp.arange(total_rows, dtype=jnp.float32)[None, :]
    ratio_rise = jnp.expm1((rows + 1.0) * log_ratio[:, None])
    ratio_next = jnp.expm1((rows + 2.0) * log_ratio[:, None])
    return ratio_rise / (ratio_next * upper[:, None])


def carried_over(line, gains, place, count, reverse):
    step = -1 if reverse else 1
    total = jnp.zeros_like(line)
    factor = jnp.ones_like(gains[0])
    for hop in range(1, count):
        pairs = [(i, i + step * hop) for i in range(count) if 0 <= i + step * hop < count]
        arrived = lax.ppermute(line, "gy", pairs)
        total = total + factor[:, None, None] * arrived
        between = jnp.clip(place - step * hop, 0, count - 1)
        factor = factor * lax.dynamic_index_in_dim(gains, between, 0, False)
    return total


def wall_carries(explicit, viscous):
    row_count = explicit.shape[2]
    count = lax.axis_size("gy")
    place = lax.axis_index("gy")
    total_rows = row_count * count
    all_pivots = wall_pivots(viscous, total_rows)
    all_log_gain = jnp.log(viscous[:, None] * all_pivots).reshape(viscous.shape[0], count, row_count)
    gains = jnp.exp(jnp.sum(all_log_gain, axis=2)).T
    pivots = lax.dynamic_index_in_dim(all_pivots.reshape(-1, count, row_count), place, 1, False)
    log_gain = lax.dynamic_index_in_dim(all_log_gain, place, 1, False)
    inclusive = jnp.cumsum(log_gain, axis=1)
    exclusive = inclusive - log_gain
    row_index = jnp.arange(row_count)[:, None]
    col_index = jnp.arange(row_count)[None, :]
    lower_mask = col_index <= row_index
    upper_mask = col_index >= row_index
    spread = inclusive[:, :, None] - inclusive[:, None, :]
    forward_table = jnp.where(
        lower_mask, pivots[:, None, :] * jnp.exp(jnp.where(lower_mask, spread, 0.0)), 0.0
    )
    eliminated_local = jnp.einsum("fik,fxkz->fxiz", forward_table, explicit, precision=highest)
    enter_low = carried_over(eliminated_local[:, :, -1], gains, place, count, False)
    eliminated = eliminated_local + jnp.exp(inclusive)[:, None, :, None] * enter_low[:, :, None, :]
    reach_log = exclusive[:, None, :] - exclusive[:, :, None]
    backward_table = jnp.where(upper_mask, jnp.exp(jnp.where(upper_mask, reach_log, 0.0)), 0.0)
    solved = jnp.einsum("fik,fxkz->fxiz", backward_table, eliminated, precision=highest)
    enter_high = carried_over(solved[:, :, 0], gains, place, count, True)
    trailing = jnp.exp(inclusive[:, -1:] - exclusive)
    return solved + trailing[:, None, :, None] * enter_high[:, :, None, :]


def shifted_in(array, axis, shift):
    peers = lax.axis_size(axis)
    return lax.ppermute(array, axis, [(i, (i + shift) % peers) for i in range(peers)])


def line_kernel(fields_ref, before_ref, after_ref, local_ref, moments_ref):
    length = fields_ref.shape[1]

    def plane(k):
        if k < 0:
            return before_ref[0, k + 2]
        if k >= length:
            return after_ref[0, k - length]
        return fields_ref[0, k]

    def source(i):
        return 7.0 / 9.0 * (plane(i + 1) - plane(i - 1)) + 1.0 / 36.0 * (plane(i + 2) - plane(i - 2))

    running = jnp.zeros(fields_ref.shape[2:], jnp.float32)
    for i in range(length):
        running = source(i) + root_ratio * running
        local_ref[0, i] = running
    moments_ref[0, 0] = running
    running = jnp.zeros(fields_ref.shape[2:], jnp.float32)
    for i in reversed(range(length)):
        value = source(i)
        running = value + root_ratio * running
        local_ref[0, i] = line_gain * (local_ref[0, i] + running - value)
    moments_ref[0, 1] = running


def line_local(fields, before, after):
    count, length, rows, cols = fields.shape
    block = lambda depth: pl.BlockSpec((1, depth, rows, cols), lambda f: (f, 0, 0, 0))
    size = fields.size * 4
    return pl.pallas_call(
        line_kernel,
        grid=(count,),
        in_specs=[block(length), block(2), block(2)],
        out_specs=[block(length), block(2)],
        out_shape=[
            jax.ShapeDtypeStruct(fields.shape, jnp.float32),
            jax.ShapeDtypeStruct((count, 2, rows, cols), jnp.float32),
        ],
        cost_estimate=pl.CostEstimate(flops=20 * fields.size, bytes_accessed=2 * size, transcendentals=0),
    )(fields, before, after)


def shards(fields, viscous):
    length = fields.shape[1]
    peers = lax.axis_size("gx")
    total = length * peers
    before = shifted_in(fields[:, length - 2 :], "gx", 1)
    after = shifted_in(fields[:, :2], "gx", -1)
    local, moments = line_local(fields, before, after)
    late, local, moments = lax.optimization_barrier((fields, local, moments))
    block_weight = root_ratio**length
    arrived = (
        shifted_in(moments[:, 0], "gx", 1),
        shifted_in(moments[:, 0], "gx", 2),
        shifted_in(moments[:, 1], "gx", -1),
        shifted_in(moments[:, 1], "gx", -2),
    )
    state = {"halos": span_halos(late)}
    state, arrived = lax.optimization_barrier((state, arrived))
    left = arrived[0] + block_weight * arrived[1]
    right = arrived[2] + block_weight * arrived[3]
    spans = []
    span = 2
    while span < peers:
        spans.append(span)
        span *= 2

    def inner_part(state):
        inner = span_inner(late)
        state["partial"] = late - advect * late[0] * local - advect * late[2] * inner

    def halo_part(state):
        halo_term = span_halo_term(*state["halos"], late.shape[3])
        state["partial"] = state["partial"] - advect * late[2] * halo_term

    tasks = [inner_part, halo_part]
    for span in spans:
        state, left, right = lax.optimization_barrier((state, left, right))
        from_left = shifted_in(left, "gx", span)
        from_right = shifted_in(right, "gx", -span)
        if span == spans[0]:
            tasks.pop(0)(state)
        if span == spans[-1]:
            while tasks:
                tasks.pop(0)(state)
        state, from_left, from_right = lax.optimization_barrier((state, from_left, from_right))
        weight = root_ratio ** (length * span)
        left = left + weight * from_left
        right = right + weight * from_right
    while tasks:
        tasks.pop(0)(state)
    index = jnp.arange(length, dtype=jnp.float32)
    wrap = line_gain * root_ratio / (1.0 - root_ratio**total)
    rising = signed_power(index)[None, :, None, None]
    falling = signed_power(length - 1 - index)[None, :, None, None]
    carried = wrap * (rising * left[:, None] + falling * right[:, None])
    explicit = state["partial"] - advect * fields[0] * carried
    updated = wall_carries(explicit, viscous)
    return updated


def solution(mesh):
    in_specs = (P(None, "gx", "gy", "gz"), P())
    out_specs = P(None, "gx", "gy", "gz")
    return jax.shard_map(shards, mesh=mesh, in_specs=in_specs, out_specs=out_specs, check_vma=False)
```

```python
import math

import jax
import jax.numpy as jnp
from jax import lax
from jax.experimental import pallas as pl
from jax.sharding import PartitionSpec as P

advect = 0.3
root_ratio = (-1.0 + math.sqrt(5.0) / 3.0) * 1.5
line_gain = (1.0 + root_ratio * root_ratio) / (1.0 - root_ratio * root_ratio)
highest = lax.Precision.HIGHEST


def signed_power(exponent):
    parity = jnp.mod(exponent, 2.0)
    return (1.0 - 2.0 * parity) * jnp.exp(exponent * math.log(abs(root_ratio)))


def span_weights(offset):
    weights = {1: 45.0, -1: -45.0, 2: -9.0, -2: 9.0, 3: 1.0, -3: -1.0}
    return sum((w / 60.0) * (offset == k).astype(jnp.float32) for k, w in weights.items())


def span_halos(edges):
    return shifted_in(edges[:, :, :3], "gz", 1), shifted_in(edges[:, :, 3:6], "gz", -1)

def span_inner(fields):
    lanes = jnp.arange(fields.shape[3])
    interior = span_weights(lanes[:, None] - lanes[None, :])
    return jnp.einsum("fxyw,wz->fxyz", fields, interior, precision=highest)


def span_halo_term(before, after, cols):
    lanes = jnp.arange(cols)
    halo = jnp.arange(3)
    weights = jnp.concatenate(
        [span_weights(halo[:, None] - 3 - lanes[None, :]), span_weights(halo[:, None] + cols - lanes[None, :])]
    )
    stacked = jnp.concatenate([before, after], axis=2)
    return jnp.einsum("fxcy,cz->fxyz", stacked, weights, precision=highest)

def wall_pivots(viscous, total_rows):
    root = jnp.sqrt(1.0 + 4.0 * viscous)
    upper = 0.5 * (1.0 + 2.0 * viscous + root)
    log_ratio = -2.0 * jnp.log1p((1.0 + root) / (2.0 * viscous))
    rows = jnp.arange(total_rows, dtype=jnp.float32)[None, :]
    ratio_rise = jnp.expm1((rows + 1.0) * log_ratio[:, None])
    ratio_next = jnp.expm1((rows + 2.0) * log_ratio[:, None])
    return ratio_rise / (ratio_next * upper[:, None])


def carried_over(line, gains, place, count, reverse):
    step = -1 if reverse else 1
    total = jnp.zeros_like(line)
    factor = jnp.ones_like(gains[0])
    for hop in range(1, count):
        pairs = [(i, i + step * hop) for i in range(count) if 0 <= i + step * hop < count]
        arrived = lax.ppermute(line, "gy", pairs)
        total = total + factor[:, None, None] * arrived
        between = jnp.clip(place - step * hop, 0, count - 1)
        factor = factor * lax.dynamic_index_in_dim(gains, between, 0, False)
    return total


def wall_carries(explicit, viscous):
    row_count = explicit.shape[2]
    count = lax.axis_size("gy")
    place = lax.axis_index("gy")
    total_rows = row_count * count
    all_pivots = wall_pivots(viscous, total_rows)
    all_log_gain = jnp.log(viscous[:, None] * all_pivots).reshape(viscous.shape[0], count, row_count)
    gains = jnp.exp(jnp.sum(all_log_gain, axis=2)).T
    pivots = lax.dynamic_index_in_dim(all_pivots.reshape(-1, count, row_count), place, 1, False)
    log_gain = lax.dynamic_index_in_dim(all_log_gain, place, 1, False)
    inclusive = jnp.cumsum(log_gain, axis=1)
    exclusive = inclusive - log_gain
    row_index = jnp.arange(row_count)[:, None]
    col_index = jnp.arange(row_count)[None, :]
    lower_mask = col_index <= row_index
    upper_mask = col_index >= row_index
    spread = inclusive[:, :, None] - inclusive[:, None, :]
    forward_table = jnp.where(
        lower_mask, pivots[:, None, :] * jnp.exp(jnp.where(lower_mask, spread, 0.0)), 0.0
    )
    eliminated_local = jnp.einsum("fik,fxkz->fxiz", forward_table, explicit, precision=highest)
    enter_low = carried_over(eliminated_local[:, :, -1], gains, place, count, False)
    eliminated = eliminated_local + jnp.exp(inclusive)[:, None, :, None] * enter_low[:, :, None, :]
    reach_log = exclusive[:, None, :] - exclusive[:, :, None]
    backward_table = jnp.where(upper_mask, jnp.exp(jnp.where(upper_mask, reach_log, 0.0)), 0.0)
    solved = jnp.einsum("fik,fxkz->fxiz", backward_table, eliminated, precision=highest)
    enter_high = carried_over(solved[:, :, 0], gains, place, count, True)
    trailing = jnp.exp(inclusive[:, -1:] - exclusive)
    return solved + trailing[:, None, :, None] * enter_high[:, :, None, :]


def shifted_in(array, axis, shift):
    peers = lax.axis_size(axis)
    return lax.ppermute(array, axis, [(i, (i + shift) % peers) for i in range(peers)])


def line_kernel(fields_ref, before_ref, after_ref, pick_ref, local_ref, moments_ref, edges_ref):
    length = fields_ref.shape[1]
    for i in range(length):
        edges_ref[0, i] = lax.dot_general(
            pick_ref[...], fields_ref[0, i], (((1,), (1,)), ((), ())),
            precision=highest, preferred_element_type=jnp.float32,
        )

    def plane(k):
        if k < 0:
            return before_ref[0, k + 2]
        if k >= length:
            return after_ref[0, k - length]
        return fields_ref[0, k]

    def source(i):
        return 7.0 / 9.0 * (plane(i + 1) - plane(i - 1)) + 1.0 / 36.0 * (plane(i + 2) - plane(i - 2))

    running = jnp.zeros(fields_ref.shape[2:], jnp.float32)
    for i in range(length):
        running = source(i) + root_ratio * running
        local_ref[0, i] = running
    moments_ref[0, 0] = running
    running = jnp.zeros(fields_ref.shape[2:], jnp.float32)
    for i in reversed(range(length)):
        value = source(i)
        running = value + root_ratio * running
        local_ref[0, i] = line_gain * (local_ref[0, i] + running - value)
    moments_ref[0, 1] = running


def line_local(fields, before, after):
    count, length, rows, cols = fields.shape
    block = lambda depth: pl.BlockSpec((1, depth, rows, cols), lambda f: (f, 0, 0, 0))
    lanes = jnp.arange(cols)
    halo = jnp.arange(8)
    pick = ((lanes[None, :] == cols - 3 + halo[:, None]) & (halo[:, None] < 3)) | (
        (lanes[None, :] == halo[:, None] - 3) & (halo[:, None] >= 3) & (halo[:, None] < 6)
    )
    size = fields.size * 4
    return pl.pallas_call(
        line_kernel,
        grid=(count,),
        in_specs=[block(length), block(2), block(2), pl.BlockSpec((8, cols), lambda f: (0, 0))],
        out_specs=[block(length), block(2), pl.BlockSpec((1, length, 8, rows), lambda f: (f, 0, 0, 0))],
        out_shape=[
            jax.ShapeDtypeStruct(fields.shape, jnp.float32),
            jax.ShapeDtypeStruct((count, 2, rows, cols), jnp.float32),
            jax.ShapeDtypeStruct((count, length, 8, rows), jnp.float32),
        ],
        cost_estimate=pl.CostEstimate(flops=20 * fields.size, bytes_accessed=2 * size, transcendentals=0),
    )(fields, before, after, pick.astype(jnp.float32))

def shards(fields, viscous):
    length = fields.shape[1]
    peers = lax.axis_size("gx")
    total = length * peers
    before = shifted_in(fields[:, length - 2 :], "gx", 1)
    after = shifted_in(fields[:, :2], "gx", -1)
    local, moments, edges = line_local(fields, before, after)
    late, local, moments = lax.optimization_barrier((fields, local, moments))
    block_weight = root_ratio**length
    arrived = (
        shifted_in(moments[:, 0], "gx", 1),
        shifted_in(moments[:, 0], "gx", 2),
        shifted_in(moments[:, 1], "gx", -1),
        shifted_in(moments[:, 1], "gx", -2),
    )
    state = {"halos": span_halos(edges)}
    state, arrived = lax.optimization_barrier((state, arrived))
    left = arrived[0] + block_weight * arrived[1]
    right = arrived[2] + block_weight * arrived[3]
    spans = []
    span = 2
    while span < peers:
        spans.append(span)
        span *= 2

    def inner_part(state):
        inner = span_inner(late)
        state["partial"] = late - advect * late[0] * local - advect * late[2] * inner

    def halo_part(state):
        halo_term = span_halo_term(*state["halos"], late.shape[3])
        state["partial"] = state["partial"] - advect * late[2] * halo_term

    tasks = [inner_part, halo_part]
    for span in spans:
        state, left, right = lax.optimization_barrier((state, left, right))
        from_left = shifted_in(left, "gx", span)
        from_right = shifted_in(right, "gx", -span)
        if tasks and span != spans[-1]:
            tasks.pop(0)(state)
        elif span == spans[-1]:
            while tasks:
                tasks.pop(0)(state)
        state, from_left, from_right = lax.optimization_barrier((state, from_left, from_right))
        weight = root_ratio ** (length * span)
        left = left + weight * from_left
        right = right + weight * from_right
    while tasks:
        tasks.pop(0)(state)
    index = jnp.arange(length, dtype=jnp.float32)
    wrap = line_gain * root_ratio / (1.0 - root_ratio**total)
    rising = signed_power(index)[None, :, None, None]
    falling = signed_power(length - 1 - index)[None, :, None, None]
    carried = wrap * (rising * left[:, None] + falling * right[:, None])
    explicit = state["partial"] - advect * fields[0] * carried
    updated = wall_carries(explicit, viscous)
    return updated


def solution(mesh):
    in_specs = (P(None, "gx", "gy", "gz"), P())
    out_specs = P(None, "gx", "gy", "gz")
    return jax.shard_map(shards, mesh=mesh, in_specs=in_specs, out_specs=out_specs, check_vma=False)
```

```python
import math

import jax
import jax.numpy as jnp
from jax import lax
from jax.experimental import pallas as pl
from jax.sharding import PartitionSpec as P

advect = 0.3
root_ratio = (-1.0 + math.sqrt(5.0) / 3.0) * 1.5
line_gain = (1.0 + root_ratio * root_ratio) / (1.0 - root_ratio * root_ratio)
highest = lax.Precision.HIGHEST


def signed_power(exponent):
    parity = jnp.mod(exponent, 2.0)
    return (1.0 - 2.0 * parity) * jnp.exp(exponent * math.log(abs(root_ratio)))


def span_weights(offset):
    weights = {1: 45.0, -1: -45.0, 2: -9.0, -2: 9.0, 3: 1.0, -3: -1.0}
    return sum((w / 60.0) * (offset == k).astype(jnp.float32) for k, w in weights.items())


def span_halos(edges):
    return shifted_in(edges[:, :, :3], "gz", 1), shifted_in(edges[:, :, 3:6], "gz", -1)

def span_inner(fields):
    lanes = jnp.arange(fields.shape[3])
    interior = span_weights(lanes[:, None] - lanes[None, :])
    return jnp.einsum("fxyw,wz->fxyz", fields, interior, precision=highest)


def span_halo_term(before, after, cols):
    lanes = jnp.arange(cols)
    halo = jnp.arange(3)
    weights = jnp.concatenate(
        [span_weights(halo[:, None] - 3 - lanes[None, :]), span_weights(halo[:, None] + cols - lanes[None, :])]
    )
    stacked = jnp.concatenate([before, after], axis=2)
    return jnp.einsum("fxcy,cz->fxyz", stacked, weights, precision=highest)

def wall_pivots(viscous, total_rows):
    root = jnp.sqrt(1.0 + 4.0 * viscous)
    upper = 0.5 * (1.0 + 2.0 * viscous + root)
    log_ratio = -2.0 * jnp.log1p((1.0 + root) / (2.0 * viscous))
    rows = jnp.arange(total_rows, dtype=jnp.float32)[None, :]
    ratio_rise = jnp.expm1((rows + 1.0) * log_ratio[:, None])
    ratio_next = jnp.expm1((rows + 2.0) * log_ratio[:, None])
    return ratio_rise / (ratio_next * upper[:, None])


def carried_over(line, gains, place, count, reverse):
    step = -1 if reverse else 1
    total = jnp.zeros_like(line)
    factor = jnp.ones_like(gains[0])
    for hop in range(1, count):
        pairs = [(i, i + step * hop) for i in range(count) if 0 <= i + step * hop < count]
        arrived = lax.ppermute(line, "gy", pairs)
        total = total + factor[:, None, None] * arrived
        between = jnp.clip(place - step * hop, 0, count - 1)
        factor = factor * lax.dynamic_index_in_dim(gains, between, 0, False)
    return total


def wall_carries(explicit, viscous):
    row_count = explicit.shape[2]
    count = lax.axis_size("gy")
    place = lax.axis_index("gy")
    total_rows = row_count * count
    all_pivots = wall_pivots(viscous, total_rows)
    all_log_gain = jnp.log(viscous[:, None] * all_pivots).reshape(viscous.shape[0], count, row_count)
    gains = jnp.exp(jnp.sum(all_log_gain, axis=2)).T
    pivots = lax.dynamic_index_in_dim(all_pivots.reshape(-1, count, row_count), place, 1, False)
    log_gain = lax.dynamic_index_in_dim(all_log_gain, place, 1, False)
    inclusive = jnp.cumsum(log_gain, axis=1)
    exclusive = inclusive - log_gain
    row_index = jnp.arange(row_count)[:, None]
    col_index = jnp.arange(row_count)[None, :]
    lower_mask = col_index <= row_index
    upper_mask = col_index >= row_index
    spread = inclusive[:, :, None] - inclusive[:, None, :]
    forward_table = jnp.where(
        lower_mask, pivots[:, None, :] * jnp.exp(jnp.where(lower_mask, spread, 0.0)), 0.0
    )
    eliminated_local = jnp.einsum("fik,fxkz->fxiz", forward_table, explicit, precision=highest)
    enter_low = carried_over(eliminated_local[:, :, -1], gains, place, count, False)
    eliminated = eliminated_local + jnp.exp(inclusive)[:, None, :, None] * enter_low[:, :, None, :]
    reach_log = exclusive[:, None, :] - exclusive[:, :, None]
    backward_table = jnp.where(upper_mask, jnp.exp(jnp.where(upper_mask, reach_log, 0.0)), 0.0)
    solved = jnp.einsum("fik,fxkz->fxiz", backward_table, eliminated, precision=highest)
    enter_high = carried_over(solved[:, :, 0], gains, place, count, True)
    trailing = jnp.exp(inclusive[:, -1:] - exclusive)
    return solved + trailing[:, None, :, None] * enter_high[:, :, None, :]


def shifted_in(array, axis, shift):
    peers = lax.axis_size(axis)
    return lax.ppermute(array, axis, [(i, (i + shift) % peers) for i in range(peers)])


def line_kernel(fields_ref, before_ref, after_ref, pick_ref, along_ref, across_ref, inner_ref, local_ref, moments_ref, edges_ref):
    length = fields_ref.shape[1]
    for i in range(length):
        edges_ref[0, i] = lax.dot_general(
            pick_ref[...], fields_ref[0, i], (((1,), (1,)), ((), ())),
            precision=highest, preferred_element_type=jnp.float32,
        )

    def plane(k):
        if k < 0:
            return before_ref[0, k + 2]
        if k >= length:
            return after_ref[0, k - length]
        return fields_ref[0, k]

    def source(i):
        return 7.0 / 9.0 * (plane(i + 1) - plane(i - 1)) + 1.0 / 36.0 * (plane(i + 2) - plane(i - 2))

    running = jnp.zeros(fields_ref.shape[2:], jnp.float32)
    for i in range(length):
        running = source(i) + root_ratio * running
        local_ref[0, i] = running
    moments_ref[0, 0] = running
    running = jnp.zeros(fields_ref.shape[2:], jnp.float32)
    for i in reversed(range(length)):
        value = source(i)
        running = value + root_ratio * running
        slope = line_gain * (local_ref[0, i] + running - value)
        plain = fields_ref[0, i]
        inner = jnp.dot(plain, inner_ref[...], precision=highest, preferred_element_type=jnp.float32)
        local_ref[0, i] = plain - advect * along_ref[0, i] * slope - advect * across_ref[0, i] * inner
    moments_ref[0, 1] = running


def line_local(fields, before, after):
    count, length, rows, cols = fields.shape
    block = lambda depth: pl.BlockSpec((1, depth, rows, cols), lambda f: (f, 0, 0, 0))
    lanes = jnp.arange(cols)
    halo = jnp.arange(8)
    pick = ((lanes[None, :] == cols - 3 + halo[:, None]) & (halo[:, None] < 3)) | (
        (lanes[None, :] == halo[:, None] - 3) & (halo[:, None] >= 3) & (halo[:, None] < 6)
    )
    size = fields.size * 4
    return pl.pallas_call(
        line_kernel,
        grid=(count,),
        in_specs=[
            block(length), block(2), block(2), pl.BlockSpec((8, cols), lambda f: (0, 0)),
            pl.BlockSpec((1, length, rows, cols), lambda f: (0, 0, 0, 0)),
            pl.BlockSpec((1, length, rows, cols), lambda f: (2, 0, 0, 0)),
            pl.BlockSpec((cols, cols), lambda f: (0, 0)),
        ],
        out_specs=[block(length), block(2), pl.BlockSpec((1, length, 8, rows), lambda f: (f, 0, 0, 0))],
        out_shape=[
            jax.ShapeDtypeStruct(fields.shape, jnp.float32),
            jax.ShapeDtypeStruct((count, 2, rows, cols), jnp.float32),
            jax.ShapeDtypeStruct((count, length, 8, rows), jnp.float32),
        ],
        cost_estimate=pl.CostEstimate(flops=20 * fields.size, bytes_accessed=2 * size, transcendentals=0),
    )(fields, before, after, pick.astype(jnp.float32), fields, fields, span_weights(lanes[:, None] - lanes[None, :]))

def shards(fields, viscous):
    length = fields.shape[1]
    peers = lax.axis_size("gx")
    total = length * peers
    before = shifted_in(fields[:, length - 2 :], "gx", 1)
    after = shifted_in(fields[:, :2], "gx", -1)
    local, moments, edges = line_local(fields, before, after)
    late, local, moments = lax.optimization_barrier((fields, local, moments))
    block_weight = root_ratio**length
    arrived = (
        shifted_in(moments[:, 0], "gx", 1),
        shifted_in(moments[:, 0], "gx", 2),
        shifted_in(moments[:, 1], "gx", -1),
        shifted_in(moments[:, 1], "gx", -2),
    )
    state = {"halos": span_halos(edges)}
    state, arrived = lax.optimization_barrier((state, arrived))
    left = arrived[0] + block_weight * arrived[1]
    right = arrived[2] + block_weight * arrived[3]
    spans = []
    span = 2
    while span < peers:
        spans.append(span)
        span *= 2

    def inner_part(state):
        state["partial"] = local

    def halo_part(state):
        halo_term = span_halo_term(*state["halos"], late.shape[3])
        state["partial"] = state["partial"] - advect * late[2] * halo_term

    tasks = [inner_part, halo_part]
    for span in spans:
        state, left, right = lax.optimization_barrier((state, left, right))
        from_left = shifted_in(left, "gx", span)
        from_right = shifted_in(right, "gx", -span)
        if tasks and span != spans[-1]:
            tasks.pop(0)(state)
        elif span == spans[-1]:
            while tasks:
                tasks.pop(0)(state)
        state, from_left, from_right = lax.optimization_barrier((state, from_left, from_right))
        weight = root_ratio ** (length * span)
        left = left + weight * from_left
        right = right + weight * from_right
    while tasks:
        tasks.pop(0)(state)
    index = jnp.arange(length, dtype=jnp.float32)
    wrap = line_gain * root_ratio / (1.0 - root_ratio**total)
    rising = signed_power(index)[None, :, None, None]
    falling = signed_power(length - 1 - index)[None, :, None, None]
    carried = wrap * (rising * left[:, None] + falling * right[:, None])
    explicit = state["partial"] - advect * fields[0] * carried
    updated = wall_carries(explicit, viscous)
    return updated


def solution(mesh):
    in_specs = (P(None, "gx", "gy", "gz"), P())
    out_specs = P(None, "gx", "gy", "gz")
    return jax.shard_map(shards, mesh=mesh, in_specs=in_specs, out_specs=out_specs, check_vma=False)
```
